128 devices in a mesh: item: 4 (over y_hi, core), row: 8 (over y_lo, x), col: 4 (over z).
Axes of the slice: x: 4, y: 4 (y_hi: 2, y_lo: 2; y = y_hi * 2 + y_lo), z: 4, core: 2. Of those that a mesh axis runs over, the one named last changes fastest.
Arguments:
- latents: bfloat16 [64, 64, 4, 2432], P('row', 'col', 'item'), may hold values from -6 to 6
- prompt_tokens: bfloat16 [160, 4, 2432], P('row', 'item'), may hold values from -6 to 6
- text_count: int32 [4], P('item'), may hold values from 1 to 160, as said below
- step_index: int32 [4], P('item'), may hold values from 0 to 27
- step_table: float32 [28, 6, 2432], replicated, may hold values from -3 to 3
- item_mod: float32 [4, 6, 2432], P('item'), may hold values from -3 to 3
- w_qkv: bfloat16 [2432, 3, 1536], P(None, None, 'col'), may hold values from -1 to 1
- w_kv_text: bfloat16 [2432, 2, 1536], P(None, None, 'col'), may hold values from -0.125 to 0.125
- q_gain: float32 [64], replicated, may hold values from 0.5 to 6.5
- k_gain: float32 [64], replicated, may hold values from 0.5 to 6.5
- w_out: bfloat16 [1536, 2432], P('col'), may hold values from -0.15625 to 0.15625
- w_up: bfloat16 [2432, 9728], P(None, ('item', 'col')), may hold values from -0.125 to 0.125
- w_down: bfloat16 [9728, 2432], P(('item', 'col')), may hold values from -0.0625 to 0.0625
Outputs:
- updated: bfloat16 [64, 64, 4, 2432], P('row', 'col', 'item')
The draws below stay inside these ranges and needn't reach their ends.
Inputs may be any that keep to these rules, and one draw needn't show every extreme that they name: `text_count`: some item has all 160 text tokens live.
All inputs are finite; a program needn't handle non-finite values.
Results may differ from the reference program's by a relative error of at most 0.022.
The reference program's roundings to bfloat16 on the way count: a program that leaves them out, or rounds other values in their place, can miss the bound.
Values may be sent and summed in bfloat16 or wider, within the bound.
No kernel may reach another device: no remote copies, remote signals or barrier semaphores. Data moves between devices by JAX's collectives and lax.ppermute only.
A program may use at most 192 MiB of HBM per device.

```python
import math
import jax
import jax.numpy as jnp
from jax import lax

D = 2432
HEADS = 24
HEAD_DIM = 64
ATT = 1536
FF = 9728
GH = 64
GW = 64
TXT = 160
STEPS = 28
ITEMS = 4


def draw_text_count(key, part):
    counts = jax.random.randint(key, (ITEMS,), 1, TXT + 1)
    return counts.at[0].set(TXT).astype(jnp.int32)


def base_gains(key, offset):
    logs = jax.random.uniform(jax.random.fold_in(key, offset), (HEAD_DIM,), jnp.float32, math.log(0.5), math.log(3.0))
    return jnp.exp(logs)


def draw_q_gain(key, part):
    gains = base_gains(key, 11)
    return gains


def draw_k_gain(key, part):
    gains = base_gains(key, 13)
    return gains


def draw_w_qkv(key, part):
    normal_part = jax.random.normal(jax.random.fold_in(key, 21), (D, 3, ATT), jnp.float32)
    weights = jnp.clip(normal_part, -6.0, 6.0) * (1.0 / math.sqrt(D))
    return jnp.clip(weights, -1.0, 1.0).astype(jnp.bfloat16)


def with_ends(values, own_key, smallest, largest):
    dims = values.shape
    index_at = [jax.random.randint(jax.random.fold_in(own_key, axis), (), 0, dims[axis]) for axis in range(len(dims))]
    values = values.at[tuple(index_at)].set(smallest)
    longest = dims.index(max(dims))
    index_at[longest] = (index_at[longest] + 1) % dims[longest]
    return values.at[tuple(index_at)].set(largest)


def shard_levels(stream_key, dims, split, smallest, high):
    def one(dim, parts):
        draws = jax.random.uniform(jax.random.fold_in(jax.random.fold_in(stream_key, 6), dim), (parts,), jnp.float32, smallest / len(split), high / len(split))
        return jnp.repeat(jnp.exp(draws), dims[dim] // parts).reshape((-1,) + (1,) * (len(dims) - dim - 1))

    loudness = one(*split[0])
    for cut in split[1:]:
        loudness = loudness * one(*cut)
    return loudness


def bell_draw(own_key, dims, deviation, limit, cuts=(), held_as=jnp.bfloat16):
    drawn = deviation * jax.random.normal(own_key, dims, jnp.float32)
    if cuts:
        drawn = drawn * shard_levels(own_key, dims, cuts, -0.22, 0.18)
    return jnp.clip(drawn, -limit, limit).astype(held_as)


def setup_inputs(seed: int = 0) -> dict:
    key_list = jax.random.split(jax.random.key(seed), 14)
    latents = bell_draw(key_list[0], (GH, GW, ITEMS, D), 1.0, 6.0, ((0, 8), (1, 4), (2, 4)))
    prompt_tokens = bell_draw(key_list[1], (TXT, ITEMS, D), 1.0, 6.0, ((0, 8), (1, 4)))
    text_count = draw_text_count(jax.random.fold_in(key_list[13], 71), 0)
    step_index = with_ends(jax.random.randint(key_list[3], (ITEMS,), 0, STEPS), jax.random.fold_in(key_list[3], 1), 0, STEPS - 1).astype(jnp.int32)
    step_table = bell_draw(key_list[4], (STEPS, 6, D), 0.5, 3.0, (), jnp.float32)
    item_mod = bell_draw(key_list[5], (ITEMS, 6, D), 0.5, 3.0, ((0, 4),), jnp.float32)
    w_qkv = draw_w_qkv(jax.random.fold_in(key_list[13], 71), 0)
    w_kv_text = bell_draw(key_list[7], (D, 2, ATT), D ** -0.5, 0.125, ((2, 4),))
    q_gain = draw_q_gain(jax.random.fold_in(key_list[13], 71), 0)
    k_gain = draw_k_gain(jax.random.fold_in(key_list[13], 71), 0)
    w_out = bell_draw(key_list[10], (ATT, D), ATT ** -0.5, 0.15625, ((0, 4),))
    w_up = bell_draw(key_list[11], (D, FF), D ** -0.5, 0.125, ((1, 16),))
    w_down = bell_draw(key_list[12], (FF, D), FF ** -0.5, 0.0625, ((0, 16),))
    return dict(latents=latents, prompt_tokens=prompt_tokens, text_count=text_count, step_index=step_index, step_table=step_table, item_mod=item_mod, w_qkv=w_qkv, w_kv_text=w_kv_text, q_gain=q_gain, k_gain=k_gain, w_out=w_out, w_up=w_up, w_down=w_down)


epsilon = 1e-06

def layer_norm(values):
    values = values.astype(jnp.float32)
    center = values - lax.optimization_barrier(jnp.mean(values, axis=-1, keepdims=True))
    variance = lax.optimization_barrier(jnp.mean(center * center, axis=-1, keepdims=True))
    return center * lax.rsqrt(variance + epsilon)

def rms_heads(values, gain):
    return values * lax.rsqrt(lax.optimization_barrier(jnp.mean(values * values, axis=-1, keepdims=True)) + epsilon) * gain

def reference(latents, prompt_tokens, text_count, step_index, step_table, item_mod, w_qkv, w_kv_text, q_gain, k_gain, w_out, w_up, w_down):
    modulation = step_table[step_index] + item_mod
    image_rows = jnp.transpose(latents.reshape(GH * GW, ITEMS, D), (1, 0, 2))
    text_rows = jnp.transpose(prompt_tokens, (1, 0, 2))

    def one_item(inputs):
        states, prompt, live_count, modul = inputs
        normed_one = (layer_norm(states) * (1.0 + modul[1]) + modul[0]).astype(jnp.bfloat16)
        projected = jnp.einsum('nd,dce->cne', normed_one.astype(jnp.float32), w_qkv.astype(jnp.float32))
        query = rms_heads(projected[0].reshape(GH * GW, HEADS, HEAD_DIM), q_gain).astype(jnp.bfloat16)
        key_img = rms_heads(projected[1].reshape(GH * GW, HEADS, HEAD_DIM), k_gain).astype(jnp.bfloat16)
        value_img = projected[2].astype(jnp.bfloat16).reshape(GH * GW, HEADS, HEAD_DIM)
        text_normed = layer_norm(prompt).astype(jnp.bfloat16)
        text_proj = jnp.einsum('nd,dce->cne', text_normed.astype(jnp.float32), w_kv_text.astype(jnp.float32))
        text_key = rms_heads(text_proj[0].reshape(TXT, HEADS, HEAD_DIM), k_gain).astype(jnp.bfloat16)
        text_value = text_proj[1].astype(jnp.bfloat16).reshape(TXT, HEADS, HEAD_DIM)
        keys_all = jnp.transpose(jnp.concatenate([key_img, text_key], axis=0), (1, 0, 2))
        values_all = jnp.transpose(jnp.concatenate([value_img, text_value], axis=0), (1, 0, 2))
        live = jnp.arange(TXT, dtype=jnp.int32) < live_count
        bias = jnp.concatenate([jnp.zeros((GH * GW,), jnp.float32), jnp.where(live, 0.0, -jnp.inf).astype(jnp.float32)])
        queries = jnp.transpose(query, (1, 0, 2))

        def one_head(head_inputs):
            q_head, k_head, v_head = head_inputs
            scores = jnp.dot(q_head, k_head.T, preferred_element_type=jnp.float32) * 0.125 + bias[None, :]
            row_max = lax.optimization_barrier(jnp.max(scores, axis=1, keepdims=True))
            weights = jnp.exp(scores - row_max)
            denom = lax.optimization_barrier(jnp.sum(weights, axis=1, keepdims=True))
            result = jnp.dot(weights.astype(jnp.bfloat16), v_head, preferred_element_type=jnp.float32) / denom
            return result.astype(jnp.bfloat16)
        heads_out = lax.map(one_head, (queries, keys_all, values_all))
        heads_out = jnp.transpose(heads_out, (1, 0, 2)).reshape(GH * GW, ATT)
        attn_out = jnp.dot(heads_out, w_out, preferred_element_type=jnp.float32)
        residual = (states.astype(jnp.float32) + modul[2] * attn_out).astype(jnp.bfloat16)
        normed_two = (layer_norm(residual) * (1.0 + modul[4]) + modul[3]).astype(jnp.bfloat16)
        hidden = jax.nn.gelu(jnp.dot(normed_two, w_up, preferred_element_type=jnp.float32), approximate=True).astype(jnp.bfloat16)
        mlp_sum = jnp.dot(hidden, w_down, preferred_element_type=jnp.float32)
        return (residual.astype(jnp.float32) + modul[5] * mlp_sum).astype(jnp.bfloat16)
    results = lax.map(one_item, (image_rows, text_rows, text_count, modulation))
    return jnp.transpose(results, (1, 0, 2)).reshape(GH, GW, ITEMS, D)
```

```python
import jax
import jax.numpy as jnp
from jax import lax
from jax.sharding import Mesh
from jax.sharding import PartitionSpec as P

epsilon = 1e-06
ITEM = ("ih", "ic")


def layer_norm(values):
    values = values.astype(jnp.float32)
    center = values - jnp.mean(values, axis=-1, keepdims=True)
    variance = jnp.mean(center * center, axis=-1, keepdims=True)
    return center * lax.rsqrt(variance + epsilon)


def rms_heads(values, gain):
    return values * lax.rsqrt(jnp.mean(values * values, axis=-1, keepdims=True) + epsilon) * gain


def local(
    latents,
    prompt_tokens,
    text_count,
    step_index,
    step_table,
    item_mod,
    w_qkv,
    w_kv_text,
    q_gain,
    k_gain,
    w_out,
    w_up,
    w_down,
):
    swap = [(0, 1), (1, 0)]
    other_up = lax.ppermute(w_up, "ic", swap)
    other_down = lax.ppermute(w_down, "ic", swap)

    grid_rows, grid_cols, local_items, model_width = latents.shape
    own_rows = grid_rows * grid_cols
    tokens = latents.reshape(own_rows, local_items, model_width)
    chosen = (
        step_index[:, None] == jnp.arange(step_table.shape[0], dtype=jnp.int32)[None, :]
    ).astype(jnp.float32)
    modulation = (
        jnp.einsum("is,sjd->ijd", chosen, step_table, precision=lax.Precision.HIGHEST) + item_mod
    )
    strip_rows = lax.all_gather(tokens, "col", axis=0, tiled=True)
    strip_len = strip_rows.shape[0]
    normed_one = (layer_norm(strip_rows) * (1.0 + modulation[:, 1]) + modulation[:, 0]).astype(
        jnp.bfloat16
    )
    projected = jnp.einsum("sid,dce->csie", normed_one, w_qkv, preferred_element_type=jnp.float32)
    head_cols = w_qkv.shape[2]
    local_heads = head_cols // 64
    query = rms_heads(projected[0].reshape(strip_len, local_items, local_heads, 64), q_gain).astype(
        jnp.bfloat16
    )
    key_img = (
        rms_heads(projected[1].reshape(strip_len, local_items, local_heads, 64), k_gain)
        .astype(jnp.bfloat16)
        .reshape(strip_len, local_items, head_cols)
    )
    value_img = projected[2].astype(jnp.bfloat16)
    text_len = prompt_tokens.shape[0]
    text_normed = layer_norm(prompt_tokens).astype(jnp.bfloat16)
    text_proj = jnp.einsum(
        "tid,dce->ctie", text_normed, w_kv_text, preferred_element_type=jnp.float32
    )
    text_key = (
        rms_heads(text_proj[0].reshape(text_len, local_items, local_heads, 64), k_gain)
        .astype(jnp.bfloat16)
        .reshape(text_len, local_items, head_cols)
    )
    text_value = text_proj[1].astype(jnp.bfloat16)

    piece_len = strip_len + text_len
    kv_local = jnp.stack(
        [
            jnp.concatenate([key_img, text_key], axis=0),
            jnp.concatenate([value_img, text_value], axis=0),
        ],
        axis=1,
    )
    kv_all = lax.all_gather(kv_local, "row", axis=0, tiled=True)
    n_keys = kv_all.shape[0]
    kv_all = kv_all.reshape(n_keys, 2, local_items, local_heads, 64)
    key_all = kv_all[:, 0]
    value_all = kv_all[:, 1]

    slot = jnp.arange(n_keys, dtype=jnp.int32)
    within = slot % piece_len
    text_pos = (slot // piece_len) * text_len + (within - strip_len)
    live = (within < strip_len)[:, None] | (text_pos[:, None] < text_count[None, :])
    bias = jnp.where(live, 0.0, -jnp.inf).astype(jnp.float32)

    scores = (
        jnp.einsum("sihd,kihd->ihsk", query, key_all, preferred_element_type=jnp.float32) * 0.125
    )
    scores = scores + jnp.transpose(bias)[:, None, None, :]
    row_max = jnp.max(scores, axis=-1, keepdims=True)
    probs = jnp.exp(scores - row_max)
    denom = jnp.sum(probs, axis=-1)
    accum = jnp.einsum(
        "ihsk,kihd->ihsd",
        probs.astype(jnp.bfloat16),
        value_all,
        preferred_element_type=jnp.float32,
    )
    heads_out = (accum / denom[..., None]).astype(jnp.bfloat16)
    attended = jnp.transpose(heads_out, (2, 0, 1, 3)).reshape(strip_len, local_items, head_cols)
    attn_out = lax.psum_scatter(
        jnp.einsum("sie,ed->sid", attended, w_out, preferred_element_type=jnp.float32).astype(
            jnp.bfloat16
        ),
        "col",
        scatter_dimension=0,
        tiled=True,
    ).astype(jnp.float32)
    residual = (tokens.astype(jnp.float32) + modulation[:, 2] * attn_out).astype(jnp.bfloat16)
    normed_two = (layer_norm(residual) * (1.0 + modulation[:, 4]) + modulation[:, 3]).astype(
        jnp.bfloat16
    )
    flat_rows = normed_two.reshape(own_rows * local_items, model_width)

    gathered = lax.all_gather(flat_rows, ("ih", "col"), axis=0, tiled=True)

    def half(up, down):
        hidden = jax.nn.gelu(
            jnp.dot(gathered, up, preferred_element_type=jnp.float32), approximate=True
        ).astype(jnp.bfloat16)
        return jnp.dot(hidden, down, preferred_element_type=jnp.float32)

    partial = half(w_up, w_down) + half(other_up, other_down)
    mlp_sum = lax.psum_scatter(
        partial.astype(jnp.bfloat16),
        ("ih", "col"),
        scatter_dimension=0,
        tiled=True,
    ).astype(jnp.float32)
    mlp_sum = mlp_sum.reshape(own_rows, local_items, model_width)
    updated = (residual.astype(jnp.float32) + modulation[:, 5] * mlp_sum).astype(jnp.bfloat16)
    return updated.reshape(grid_rows, grid_cols, local_items, model_width)


def solution(mesh):
    n_item = mesh.shape["item"]
    devices = mesh.devices.reshape(
        (n_item // 2, 2, mesh.shape["row"], mesh.shape["col"])
    )
    split_mesh = Mesh(devices, ("ih", "ic", "row", "col"))
    placed = (
        P("row", "col", ITEM, None),
        P("row", ITEM, None),
        P(ITEM),
        P(ITEM),
        P(),
        P(ITEM, None, None),
        P(None, None, "col"),
        P(None, None, "col"),
        P(),
        P(),
        P("col", None),
        P(None, (ITEM + ("col",))),
        P((ITEM + ("col",)), None),
    )
    return jax.shard_map(
        local,
        mesh=split_mesh,
        in_specs=placed,
        out_specs=P("row", "col", ITEM, None),
        check_vma=False,
    )
```

```python
import jax
import jax.numpy as jnp
from jax import lax
from jax.sharding import Mesh
from jax.sharding import PartitionSpec as P

epsilon = 1e-06
ITEM = ("ih", "ic")


def layer_norm(values):
    values = values.astype(jnp.float32)
    center = values - jnp.mean(values, axis=-1, keepdims=True)
    variance = jnp.mean(center * center, axis=-1, keepdims=True)
    return center * lax.rsqrt(variance + epsilon)


def rms_heads(values, gain):
    return values * lax.rsqrt(jnp.mean(values * values, axis=-1, keepdims=True) + epsilon) * gain


def local(
    latents,
    prompt_tokens,
    text_count,
    step_index,
    step_table,
    item_mod,
    w_qkv,
    w_kv_text,
    q_gain,
    k_gain,
    w_out,
    w_up,
    w_down,
):
    n_row = lax.axis_size("row")
    half_row = n_row // 2
    mirror = []
    for ih in range(2):
        for y_lo in range(2):
            for x in range(half_row):
                mirror.append(
                    (ih * n_row + y_lo * half_row + x, (1 - ih) * n_row + (1 - y_lo) * half_row + x)
                )
    other_up = lax.ppermute(w_up, ("ih", "row"), mirror)
    other_down = lax.ppermute(w_down, ("ih", "row"), mirror)

    grid_rows, grid_cols, local_items, model_width = latents.shape
    own_rows = grid_rows * grid_cols
    tokens = latents.reshape(own_rows, local_items, model_width)
    chosen = (
        step_index[:, None] == jnp.arange(step_table.shape[0], dtype=jnp.int32)[None, :]
    ).astype(jnp.float32)
    modulation = (
        jnp.einsum("is,sjd->ijd", chosen, step_table, precision=lax.Precision.HIGHEST) + item_mod
    )
    strip_rows = lax.all_gather(tokens, "col", axis=0, tiled=True)
    strip_len = strip_rows.shape[0]
    normed_one = (layer_norm(strip_rows) * (1.0 + modulation[:, 1]) + modulation[:, 0]).astype(
        jnp.bfloat16
    )
    projected = jnp.einsum("sid,dce->csie", normed_one, w_qkv, preferred_element_type=jnp.float32)
    head_cols = w_qkv.shape[2]
    local_heads = head_cols // 64
    query = rms_heads(projected[0].reshape(strip_len, local_items, local_heads, 64), q_gain).astype(
        jnp.bfloat16
    )
    key_img = (
        rms_heads(projected[1].reshape(strip_len, local_items, local_heads, 64), k_gain)
        .astype(jnp.bfloat16)
        .reshape(strip_len, local_items, head_cols)
    )
    value_img = projected[2].astype(jnp.bfloat16)
    text_len = prompt_tokens.shape[0]
    text_normed = layer_norm(prompt_tokens).astype(jnp.bfloat16)
    text_proj = jnp.einsum(
        "tid,dce->ctie", text_normed, w_kv_text, preferred_element_type=jnp.float32
    )
    text_key = (
        rms_heads(text_proj[0].reshape(text_len, local_items, local_heads, 64), k_gain)
        .astype(jnp.bfloat16)
        .reshape(text_len, local_items, head_cols)
    )
    text_value = text_proj[1].astype(jnp.bfloat16)

    text_slots = -(-text_len // 16) * 16
    piece_len = strip_len + text_slots
    pad = jnp.zeros((text_slots - text_len, local_items, head_cols), jnp.bfloat16)
    kv_local = jnp.concatenate([key_img, text_key, pad, value_img, text_value, pad], axis=0)
    kv_all = lax.all_gather(kv_local, "row", axis=0, tiled=True)
    kv_all, other_up = lax.optimization_barrier((kv_all, other_up))
    kv_all = kv_all.reshape(n_row, 2, piece_len, local_items, local_heads, 64)
    n_keys = n_row * piece_len
    key_all = kv_all[:, 0].reshape(n_keys, local_items, local_heads, 64)
    value_all = kv_all[:, 1].reshape(n_keys, local_items, local_heads, 64)

    slot = jnp.arange(n_keys, dtype=jnp.int32)
    within = slot % piece_len
    text_pos = (slot // piece_len) * text_len + (within - strip_len)
    is_text = (within >= strip_len) & (within < strip_len + text_len)
    live = (within < strip_len)[:, None] | (
        is_text[:, None] & (text_pos[:, None] < text_count[None, :])
    )
    bias = jnp.where(live, 0.0, -jnp.inf).astype(jnp.float32)

    scores = (
        jnp.einsum("sihd,kihd->ihsk", query, key_all, preferred_element_type=jnp.float32) * 0.125
    )
    scores = scores + jnp.transpose(bias)[:, None, None, :]
    row_max = jnp.max(scores, axis=-1, keepdims=True)
    probs = jnp.exp(scores - row_max)
    denom = jnp.sum(probs, axis=-1)
    accum = jnp.einsum(
        "ihsk,kihd->ihsd",
        probs.astype(jnp.bfloat16),
        value_all,
        preferred_element_type=jnp.float32,
    )
    heads_out = (accum / denom[..., None]).astype(jnp.bfloat16)
    attended = jnp.transpose(heads_out, (2, 0, 1, 3)).reshape(strip_len, local_items, head_cols)
    attended, other_down = lax.optimization_barrier((attended, other_down))
    attn_out = lax.psum_scatter(
        jnp.einsum("sie,ed->sid", attended, w_out, preferred_element_type=jnp.float32).astype(
            jnp.bfloat16
        ),
        "col",
        scatter_dimension=0,
        tiled=True,
    ).astype(jnp.float32)
    residual = (tokens.astype(jnp.float32) + modulation[:, 2] * attn_out).astype(jnp.bfloat16)
    normed_two = (layer_norm(residual) * (1.0 + modulation[:, 4]) + modulation[:, 3]).astype(
        jnp.bfloat16
    )
    flat_rows = normed_two.reshape(own_rows * local_items, model_width)

    gathered = lax.all_gather(flat_rows, ("ic", "col"), axis=0, tiled=True)

    def half(up, down):
        hidden = jax.nn.gelu(
            jnp.dot(gathered, up, preferred_element_type=jnp.float32), approximate=True
        ).astype(jnp.bfloat16)
        return jnp.dot(hidden, down, preferred_element_type=jnp.float32)

    partial = half(w_up, w_down) + half(other_up, other_down)
    mlp_sum = lax.psum_scatter(
        partial.astype(jnp.bfloat16),
        ("ic", "col"),
        scatter_dimension=0,
        tiled=True,
    ).astype(jnp.float32)
    mlp_sum = mlp_sum.reshape(own_rows, local_items, model_width)
    updated = (residual.astype(jnp.float32) + modulation[:, 5] * mlp_sum).astype(jnp.bfloat16)
    return updated.reshape(grid_rows, grid_cols, local_items, model_width)


def solution(mesh):
    n_item = mesh.shape["item"]
    devices = mesh.devices.reshape(
        (n_item // 2, 2, mesh.shape["row"], mesh.shape["col"])
    )
    split_mesh = Mesh(devices, ("ih", "ic", "row", "col"))
    placed = (
        P("row", "col", ITEM, None),
        P("row", ITEM, None),
        P(ITEM),
        P(ITEM),
        P(),
        P(ITEM, None, None),
        P(None, None, "col"),
        P(None, None, "col"),
        P(),
        P(),
        P("col", None),
        P(None, (ITEM + ("col",))),
        P((ITEM + ("col",)), None),
    )
    return jax.shard_map(
        local,
        mesh=split_mesh,
        in_specs=placed,
        out_specs=P("row", "col", ITEM, None),
        check_vma=False,
    )
```

```python
import jax
import jax.numpy as jnp
from jax import lax
from jax.experimental import pallas as pl
from jax.experimental.pallas import tpu as pltpu
from jax.sharding import Mesh
from jax.sharding import PartitionSpec as P

epsilon = 1e-06
ITEM = ("ih", "ic")


def layer_norm(values):
    values = values.astype(jnp.float32)
    center = values - jnp.mean(values, axis=-1, keepdims=True)
    variance = jnp.mean(center * center, axis=-1, keepdims=True)
    return center * lax.rsqrt(variance + epsilon)


def rms_heads(values, gain):
    return values * lax.rsqrt(jnp.mean(values * values, axis=-1, keepdims=True) + epsilon) * gain


def attention_kernel(q_ref, *refs):
    kv_refs = refs[:-3]
    bias_ref, o_ref, s_scr = refs[-3:]
    n_strip = len(kv_refs)
    width = q_ref.shape[1]
    piece = s_scr.shape[2]
    q = q_ref[...]
    tq = q.shape[0]
    lane = lax.broadcasted_iota(jnp.int32, (tq, width), 1)
    half = width // 2
    outs = []
    for parity in range(2):
        own = (lane >= parity * half) & (lane < (parity + 1) * half)
        q_one = jnp.where(own, q, jnp.zeros_like(q))
        row_max = jnp.full((tq, 1), -jnp.inf, jnp.float32)
        for r in range(n_strip):
            keys = kv_refs[r][0:piece, :]
            s = lax.dot_general(q_one, keys, (((1,), (1,)), ((), ())),
                                preferred_element_type=jnp.float32)
            s = s * 0.125 + bias_ref[r:r + 1, :]
            s_scr[r] = s
            row_max = jnp.maximum(row_max, jnp.max(s, axis=1, keepdims=True))
        denom = jnp.zeros((tq, 1), jnp.float32)
        acc = jnp.zeros((tq, width), jnp.float32)
        for r in range(n_strip):
            w = jnp.exp(s_scr[r] - row_max)
            denom = denom + jnp.sum(w, axis=1, keepdims=True)
            acc = acc + jnp.dot(w.astype(jnp.bfloat16), kv_refs[r][piece:2 * piece, :],
                                preferred_element_type=jnp.float32)
        outs.append(acc / denom)
    o_ref[...] = jnp.where(lane < half, outs[0], outs[1]).astype(o_ref.dtype)


def attention(query, kv_parts, bias, tq=512):
    S, C = query.shape
    two_piece = kv_parts[0].shape[0]
    piece = two_piece // 2
    R = len(kv_parts)
    pairs = C // 128
    return pl.pallas_call(
        attention_kernel,
        out_shape=jax.ShapeDtypeStruct((S, C), jnp.bfloat16),
        grid=(pairs, S // tq),
        in_specs=[pl.BlockSpec((tq, 128), lambda h, i: (i, h))]
        + [pl.BlockSpec((two_piece, 128), lambda h, i: (0, h)) for _ in range(R)]
        + [pl.BlockSpec((R, piece), lambda h, i: (0, 0))],
        out_specs=pl.BlockSpec((tq, 128), lambda h, i: (i, h)),
        scratch_shapes=[pltpu.VMEM((R, tq, piece), jnp.float32)],
    )(query, *kv_parts, bias)


def local(
    latents,
    prompt_tokens,
    text_count,
    step_index,
    step_table,
    item_mod,
    w_qkv,
    w_kv_text,
    q_gain,
    k_gain,
    w_out,
    w_up,
    w_down,
):
    n_row = lax.axis_size("row")
    half_row = n_row // 2
    mirror = []
    for ih in range(2):
        for y_lo in range(2):
            for x in range(half_row):
                mirror.append(
                    (ih * n_row + y_lo * half_row + x, (1 - ih) * n_row + (1 - y_lo) * half_row + x)
                )
    other_up = lax.ppermute(w_up, ("ih", "row"), mirror)
    down_rows = w_down.shape[0] // 2
    other_down_a = lax.ppermute(w_down[:down_rows], ("ih", "row"), mirror)
    other_down_b = lax.ppermute(w_down[down_rows:], ("ih", "row"), mirror)

    grid_rows, grid_cols, local_items, model_width = latents.shape
    own_rows = grid_rows * grid_cols
    tokens = latents.reshape(own_rows, local_items, model_width)
    chosen = (
        step_index[:, None] == jnp.arange(step_table.shape[0], dtype=jnp.int32)[None, :]
    ).astype(jnp.float32)
    modulation = (
        jnp.einsum("is,sjd->ijd", chosen, step_table, precision=lax.Precision.HIGHEST) + item_mod
    )
    strip_rows = lax.all_gather(tokens, "col", axis=0, tiled=True)
    strip_len = strip_rows.shape[0]
    normed_one = (layer_norm(strip_rows) * (1.0 + modulation[:, 1]) + modulation[:, 0]).astype(
        jnp.bfloat16
    )
    projected = jnp.einsum("sid,dce->csie", normed_one, w_qkv, preferred_element_type=jnp.float32)
    head_cols = w_qkv.shape[2]
    local_heads = head_cols // 64
    query = rms_heads(projected[0].reshape(strip_len, local_items, local_heads, 64), q_gain).astype(
        jnp.bfloat16
    )
    key_img = (
        rms_heads(projected[1].reshape(strip_len, local_items, local_heads, 64), k_gain)
        .astype(jnp.bfloat16)
        .reshape(strip_len, local_items, head_cols)
    )
    value_img = projected[2].astype(jnp.bfloat16)
    text_len = prompt_tokens.shape[0]
    text_normed = layer_norm(prompt_tokens).astype(jnp.bfloat16)
    text_proj = jnp.einsum(
        "tid,dce->ctie", text_normed, w_kv_text, preferred_element_type=jnp.float32
    )
    text_key = (
        rms_heads(text_proj[0].reshape(text_len, local_items, local_heads, 64), k_gain)
        .astype(jnp.bfloat16)
        .reshape(text_len, local_items, head_cols)
    )
    text_value = text_proj[1].astype(jnp.bfloat16)

    text_slots = -(-text_len // 16) * 16
    piece_len = strip_len + text_slots
    flat_kv = [
        part.reshape(part.shape[0], local_items * head_cols)
        for part in (key_img, text_key, value_img, text_value)
    ]
    pad = jnp.zeros((text_slots - text_len, local_items * head_cols), jnp.bfloat16)
    kv_local = jnp.concatenate(
        [flat_kv[0], flat_kv[1], pad, flat_kv[2], flat_kv[3], pad], axis=0
    )
    me = lax.axis_index("row")
    kv_parts = [kv_local] + [
        lax.ppermute(kv_local, "row", [(i, (i + k) % n_row) for i in range(n_row)])
        for k in range(1, n_row)
    ]
    kv_parts, other_up = lax.optimization_barrier((kv_parts, other_up))

    within = jnp.arange(piece_len, dtype=jnp.int32)[None, :]
    strip_of = (me - jnp.arange(n_row, dtype=jnp.int32)) % n_row
    text_pos = strip_of[:, None] * text_len + (within - strip_len)
    live = (within < strip_len) | (
        (within < strip_len + text_len) & (text_pos < text_count[0])
    )
    bias = jnp.where(live, 0.0, -jnp.inf).astype(jnp.float32)

    heads_out = attention(query.reshape(strip_len, head_cols), kv_parts, bias)
    heads_out, other_down_a = lax.optimization_barrier((heads_out, other_down_a))
    attended = heads_out.reshape(strip_len, local_items, head_cols)
    attn_out = lax.psum_scatter(
        jnp.einsum("sie,ed->sid", attended, w_out, preferred_element_type=jnp.float32).astype(
            jnp.bfloat16
        ),
        "col",
        scatter_dimension=0,
        tiled=True,
    ).astype(jnp.float32)
    attn_out, other_down_b = lax.optimization_barrier((attn_out, other_down_b))
    other_down = jnp.concatenate([other_down_a, other_down_b], axis=0)
    residual = (tokens.astype(jnp.float32) + modulation[:, 2] * attn_out).astype(jnp.bfloat16)
    normed_two = (layer_norm(residual) * (1.0 + modulation[:, 4]) + modulation[:, 3]).astype(
        jnp.bfloat16
    )
    flat_rows = normed_two.reshape(own_rows * local_items, model_width)

    gathered = lax.all_gather(flat_rows, ("ic", "col"), axis=0, tiled=True)

    def half(up, down):
        hidden = jax.nn.gelu(
            jnp.dot(gathered, up, preferred_element_type=jnp.float32), approximate=True
        ).astype(jnp.bfloat16)
        return jnp.dot(hidden, down, preferred_element_type=jnp.float32)

    partial = half(w_up, w_down) + half(other_up, other_down)
    chip_sum = lax.psum_scatter(
        partial.astype(jnp.bfloat16), "ic", scatter_dimension=0, tiled=True
    )
    mlp_sum = lax.psum_scatter(chip_sum, "col", scatter_dimension=0, tiled=True).astype(
        jnp.float32
    )
    mlp_sum = mlp_sum.reshape(own_rows, local_items, model_width)
    updated = (residual.astype(jnp.float32) + modulation[:, 5] * mlp_sum).astype(jnp.bfloat16)
    return updated.reshape(grid_rows, grid_cols, local_items, model_width)


def solution(mesh):
    n_item = mesh.shape["item"]
    devices = mesh.devices.reshape(
        (n_item // 2, 2, mesh.shape["row"], mesh.shape["col"])
    )
    split_mesh = Mesh(devices, ("ih", "ic", "row", "col"))
    placed = (
        P("row", "col", ITEM, None),
        P("row", ITEM, None),
        P(ITEM),
        P(ITEM),
        P(),
        P(ITEM, None, None),
        P(None, None, "col"),
        P(None, None, "col"),
        P(),
        P(),
        P("col", None),
        P(None, (ITEM + ("col",))),
        P((ITEM + ("col",)), None),
    )
    return jax.shard_map(
        local,
        mesh=split_mesh,
        in_specs=placed,
        out_specs=P("row", "col", ITEM, None),
        check_vma=False,
    )
```
